512 devices in a mesh: ctx: 64 (over z, y_hi, core), head: 8 (over y_lo, x).
Axes of the slice: x: 4, y: 8 (y_hi: 4, y_lo: 2; y = y_hi * 2 + y_lo), z: 8, core: 2. Of those that a mesh axis runs over, the one named last changes fastest.
Arguments:
- queries_cross: bfloat16 [8192, 3072], P('ctx', 'head'), may hold values from -38 to 38
- outputs_grad: bfloat16 [8192, 3072], P('ctx', 'head'), may hold values from -3 to 3
- keys_shared: bfloat16 [8192, 1024], P('ctx', 'head'), may hold values from -5 to 5
- values_shared: bfloat16 [8192, 1024], P('ctx', 'head'), may hold values from -6 to 6
- stripe_order: int32 [8192], replicated, may hold values from 0 to 8191, as said below
- segments: int32 [8192], replicated, may hold values from 0 to 7, as said below
- norm_input: bfloat16 [8192, 3072], P('ctx', 'head'), may hold values from -70 to 70
- norm_gain: float32 [3072], replicated, may hold values from 0.1 to 1.9
- weight_key: bfloat16 [3072, 1024], P(None, 'head'), may hold values from -0.109375 to 0.109375
- weight_value: bfloat16 [3072, 1024], P(None, 'head'), may hold values from -0.109375 to 0.109375
- upstream: bfloat16 [8192, 3072], P('ctx', 'head'), may hold values from -1.5 to 1.5
- weight_out: bfloat16 [3072, 3072], P('head'), may hold values from -0.109375 to 0.109375
- queries_window: bfloat16 [8192, 3072], P('ctx', 'head'), may hold values from -38 to 38
- keys_window: bfloat16 [8192, 1024], P('ctx', 'head'), may hold values from -5 to 5
- values_window: bfloat16 [8192, 1024], P('ctx', 'head'), may hold values from -6 to 6
Outputs:
- grad_cross: bfloat16 [8192, 3072], P('ctx', 'head')
- grad_stream: bfloat16 [8192, 3072], P('ctx', 'head')
- grad_queries: bfloat16 [8192, 3072], P('ctx', 'head')
- grad_keys: bfloat16 [8192, 1024], P('ctx', 'head')
- grad_values: bfloat16 [8192, 1024], P('ctx', 'head')
The draws below stay inside these ranges and needn't reach their ends.
Inputs may be any that keep to these rules, and one draw needn't show every extreme that they name: `stripe_order`: a permutation of all positions; the row at index c * 128 + s holds a position from s * (64) to s * 64 + 8192 // 128 - 1. `segments`: starts at 0, never falls, rises by at most one from a position to the next.
All inputs are finite; a program needn't handle non-finite values.
Results may differ from the reference program's by a relative error of at most 0.022.
Values may be sent and summed in bfloat16 or wider, within the bound.
No kernel may reach another device: no remote copies, remote signals or barrier semaphores. Data moves between devices by JAX's collectives and lax.ppermute only.
A program may use at most 128 MiB of HBM per device.

```python
import math
import jax
import jax.numpy as jnp
from jax import lax

D = 3072
HEADS = 24
KV_HEADS = 8
HEAD_DIM = 128
WINDOW = 1024
ROWS = 128
TOKENS = 8192
DOCS = 8


def stripe_table(key):
    devices = TOKENS // ROWS
    row_keys = jax.random.split(jax.random.fold_in(key, 3), ROWS)
    orders = jax.vmap(lambda single: jax.random.permutation(single, devices))(row_keys)
    stripes = jnp.arange(ROWS, dtype=jnp.int32)[:, None] * devices + orders.astype(jnp.int32)
    return stripes.T.reshape(TOKENS)


def segment_table(key):
    cut_places = jax.random.permutation(jax.random.fold_in(key, 4), TOKENS - 1)[:DOCS - 1] + 1
    boundary = jnp.zeros((TOKENS,), jnp.int32).at[cut_places].set(1)
    return jnp.cumsum(boundary).astype(jnp.int32)


def base_values(key, salt_value, column_total):
    folded_key = jax.random.fold_in(key, salt_value)
    base_draw = jnp.clip(jax.random.normal(folded_key, (TOKENS, column_total), jnp.float32), -5.0, 5.0)
    return base_draw


def draw_stripe_order(key, part):
    return stripe_table(key)


def draw_segments(key, part):
    return segment_table(key)


def draw_keys_shared(key, part):
    base_draw = base_values(key, 1, KV_HEADS * HEAD_DIM)
    return base_draw.astype(jnp.bfloat16)


def draw_queries_cross(key, part):
    base_draw = base_values(key, 2, HEADS * HEAD_DIM)
    return base_draw.astype(jnp.bfloat16)


def draw_keys_window(key, part):
    base_draw = base_values(key, 5, KV_HEADS * HEAD_DIM)
    return base_draw.astype(jnp.bfloat16)


def draw_queries_window(key, part):
    base_draw = base_values(key, 6, HEADS * HEAD_DIM)
    return base_draw.astype(jnp.bfloat16)


def draw_norm_input(key, part):
    row_scale = jnp.exp(jax.random.uniform(jax.random.fold_in(key, 7), (TOKENS, 1), jnp.float32, math.log(0.1), 0.0))
    column_ramp = jnp.exp(0.5 * math.log(3.0) * jnp.arange(D, dtype=jnp.float32) / (D - 1))
    column_scale = column_ramp * jnp.exp(jax.random.uniform(jax.random.fold_in(key, 8), (D,), jnp.float32, 0.0, math.log(10.0)))
    base_draw = jnp.clip(jax.random.normal(jax.random.fold_in(key, 10), (TOKENS, D), jnp.float32), -4.0, 4.0)
    return (row_scale * column_scale[None, :] * base_draw).astype(jnp.bfloat16)


def levels(rng, dims, cuts, least, largest):
    gain = 1.0
    for dim, parts in cuts:
        steps = jax.random.uniform(jax.random.fold_in(jax.random.fold_in(rng, 6), dim), (parts,), jnp.float32, least / len(cuts), largest / len(cuts))
        gain = gain * jnp.repeat(jnp.exp(steps), dims[dim] // parts).reshape((-1,) + (1,) * (len(dims) - 1 - dim))
    return gain


def bell_draw(key, shape, scale, reach, cuts=(), held_as=jnp.bfloat16):
    array = scale * jax.random.normal(key, shape, jnp.float32)
    if cuts:
        array = array * levels(key, shape, cuts, -0.22, 0.18)
    return jnp.clip(array, -reach, reach).astype(held_as)


def setup_inputs(seed: int = 0) -> dict:
    arg_keys = jax.random.split(jax.random.key(seed), 16)
    return {
        "queries_cross": draw_queries_cross(jax.random.fold_in(arg_keys[15], 71), 0),
        "outputs_grad": bell_draw(arg_keys[1], (TOKENS, D), 0.5, 3.0, ((0, 64), (1, 8))),
        "keys_shared": draw_keys_shared(jax.random.fold_in(arg_keys[15], 71), 0),
        "values_shared": bell_draw(arg_keys[3], (TOKENS, KV_HEADS * HEAD_DIM), 1.0, 6.0, ((0, 64), (1, 8))),
        "stripe_order": draw_stripe_order(jax.random.fold_in(arg_keys[15], 71), 0),
        "segments": draw_segments(jax.random.fold_in(arg_keys[15], 71), 0),
        "norm_input": draw_norm_input(jax.random.fold_in(arg_keys[15], 71), 0),
        "norm_gain": jnp.clip(1.0 + 0.18 * jax.random.normal(arg_keys[7], (D,), jnp.float32), 0.1, 1.9),
        "weight_key": bell_draw(arg_keys[8], (D, KV_HEADS * HEAD_DIM), D ** -0.5, 0.109375, ((1, 8),)),
        "weight_value": bell_draw(arg_keys[9], (D, KV_HEADS * HEAD_DIM), D ** -0.5, 0.109375, ((1, 8),)),
        "upstream": bell_draw(arg_keys[10], (TOKENS, D), 0.25, 1.5, ((0, 64), (1, 8))),
        "weight_out": bell_draw(arg_keys[11], (D, D), D ** -0.5, 0.109375, ((0, 8),)),
        "queries_window": draw_queries_window(jax.random.fold_in(arg_keys[15], 71), 0),
        "keys_window": draw_keys_window(jax.random.fold_in(arg_keys[15], 71), 0),
        "values_window": bell_draw(arg_keys[14], (TOKENS, KV_HEADS * HEAD_DIM), 1.0, 6.0, ((0, 64), (1, 8))),
    }


def inverse_of(permutation):
    length = permutation.shape[0]
    return jnp.zeros((length,), jnp.int32).at[permutation].set(jnp.arange(length, dtype=jnp.int32))

def attend_back(queries, out_grads, keys, values, allowed):
    factor = HEAD_DIM ** (-0.5)
    query_wide = queries.astype(jnp.float32)
    grad_wide = out_grads.astype(jnp.float32)
    key_wide = keys.astype(jnp.float32)
    value_wide = values.astype(jnp.float32)
    scores = jnp.einsum('jbe,ke->jbk', query_wide, key_wide) * factor
    scores = jnp.where(allowed[None], scores, -jnp.inf)
    row_peak = lax.optimization_barrier(jnp.max(scores, axis=2, keepdims=True))
    logsum = row_peak + jnp.log(lax.optimization_barrier(jnp.sum(jnp.exp(scores - row_peak), axis=2, keepdims=True)))
    weights = jnp.exp(scores - logsum)
    weights_low = weights.astype(jnp.bfloat16)
    output = jnp.einsum('jbk,ke->jbe', weights_low.astype(jnp.float32), value_wide)
    row_inner = lax.optimization_barrier(jnp.sum(grad_wide * output, axis=2, keepdims=True))
    weight_grads = jnp.einsum('jbe,ke->jbk', grad_wide, value_wide)
    score_grads = (weights * (weight_grads - row_inner)).astype(jnp.bfloat16).astype(jnp.float32)
    query_grad = jnp.einsum('jbk,ke->jbe', score_grads, key_wide) * factor
    key_grad = jnp.einsum('jbk,jbe->ke', score_grads, query_wide) * factor
    value_grad = jnp.einsum('jbk,jbe->ke', weights_low.astype(jnp.float32), grad_wide)
    return (query_grad, key_grad, value_grad)

def cross_section(queries_cross, outputs_grad, keys_shared, values_shared, stripe_order, segments):
    key_count = queries_cross.shape[0]
    row_block = min(512, key_count)
    group_size = HEADS // KV_HEADS
    block_count = key_count // row_block
    query_heads = queries_cross.reshape(key_count, KV_HEADS, group_size, HEAD_DIM).transpose(1, 2, 0, 3)
    grad_heads = outputs_grad.reshape(key_count, KV_HEADS, group_size, HEAD_DIM).transpose(1, 2, 0, 3)
    key_heads = keys_shared.reshape(key_count, KV_HEADS, HEAD_DIM).transpose(1, 0, 2)
    value_heads = values_shared.reshape(key_count, KV_HEADS, HEAD_DIM).transpose(1, 0, 2)
    key_segment = segments[stripe_order]

    def per_head(operands):
        query_all, grad_all, key_all, value_all = operands

        def block_step(running, block_index):
            first_row = block_index * row_block
            query_block = lax.dynamic_slice_in_dim(query_all, first_row, row_block, 1)
            grad_block = lax.dynamic_slice_in_dim(grad_all, first_row, row_block, 1)
            query_place = lax.dynamic_slice_in_dim(stripe_order, first_row, row_block)
            query_segment = lax.dynamic_slice_in_dim(key_segment, first_row, row_block)
            allowed = (stripe_order[None, :] <= query_place[:, None]) & (key_segment[None, :] == query_segment[:, None])
            query_grad, key_grad, value_grad = attend_back(query_block, grad_block, key_all, value_all, allowed)
            return ((running[0] + key_grad, running[1] + value_grad), query_grad)
        empty_sums = jnp.zeros((key_count, HEAD_DIM), jnp.float32)
        sums, query_grads = lax.scan(block_step, (empty_sums, empty_sums), jnp.arange(block_count, dtype=jnp.int32))
        return (query_grads.transpose(1, 0, 2, 3).reshape(group_size, key_count, HEAD_DIM), sums[0], sums[1])
    query_grad, key_grad, value_grad = lax.map(per_head, (query_heads, grad_heads, key_heads, value_heads))
    grad_cross = query_grad.transpose(2, 0, 1, 3).reshape(key_count, HEADS * HEAD_DIM).astype(jnp.bfloat16)
    key_out = key_grad.transpose(1, 0, 2).reshape(key_count, KV_HEADS * HEAD_DIM).astype(jnp.bfloat16)
    value_out = value_grad.transpose(1, 0, 2).reshape(key_count, KV_HEADS * HEAD_DIM).astype(jnp.bfloat16)
    return (grad_cross, key_out, value_out)

def window_section(queries_window, head_grads, keys_window, values_window, segments):
    key_count = queries_window.shape[0]
    row_block = min(512, key_count)
    group_size = HEADS // KV_HEADS
    block_count = key_count // row_block
    span = WINDOW + row_block
    query_heads = queries_window.reshape(key_count, KV_HEADS, group_size, HEAD_DIM).transpose(1, 2, 0, 3)
    grad_heads = head_grads.reshape(key_count, KV_HEADS, group_size, HEAD_DIM).transpose(1, 2, 0, 3)
    front = jnp.zeros((WINDOW, KV_HEADS * HEAD_DIM), jnp.bfloat16)
    key_heads = jnp.concatenate([front, keys_window], axis=0).reshape(WINDOW + key_count, KV_HEADS, HEAD_DIM).transpose(1, 0, 2)
    value_heads = jnp.concatenate([front, values_window], axis=0).reshape(WINDOW + key_count, KV_HEADS, HEAD_DIM).transpose(1, 0, 2)
    padded = jnp.concatenate([jnp.full((WINDOW,), -1, jnp.int32), segments.astype(jnp.int32)])

    def per_head(operands):
        query_all, grad_all, key_all, value_all = operands

        def block_step(running, block_index):
            first_row = block_index * row_block
            query_block = lax.dynamic_slice_in_dim(query_all, first_row, row_block, 1)
            grad_block = lax.dynamic_slice_in_dim(grad_all, first_row, row_block, 1)
            key_block = lax.dynamic_slice_in_dim(key_all, first_row, span, 0)
            value_block = lax.dynamic_slice_in_dim(value_all, first_row, span, 0)
            query_place = first_row + jnp.arange(row_block, dtype=jnp.int32)
            key_place = first_row - WINDOW + jnp.arange(span, dtype=jnp.int32)
            key_segment = lax.dynamic_slice_in_dim(padded, first_row, span)
            query_segment = lax.dynamic_slice_in_dim(segments.astype(jnp.int32), first_row, row_block)
            allowed = (key_place[None, :] <= query_place[:, None]) & (key_place[None, :] > query_place[:, None] - WINDOW) & (key_segment[None, :] == query_segment[:, None])
            query_grad, key_grad, value_grad = attend_back(query_block, grad_block, key_block, value_block, allowed)
            key_sum = lax.dynamic_update_slice_in_dim(running[0], lax.dynamic_slice_in_dim(running[0], first_row, span, 0) + key_grad, first_row, 0)
            value_sum = lax.dynamic_update_slice_in_dim(running[1], lax.dynamic_slice_in_dim(running[1], first_row, span, 0) + value_grad, first_row, 0)
            return ((key_sum, value_sum), query_grad)
        empty_sums = jnp.zeros((WINDOW + key_count, HEAD_DIM), jnp.float32)
        sums, query_grads = lax.scan(block_step, (empty_sums, empty_sums), jnp.arange(block_count, dtype=jnp.int32))
        return (query_grads.transpose(1, 0, 2, 3).reshape(group_size, key_count, HEAD_DIM), sums[0][WINDOW:], sums[1][WINDOW:])
    query_grad, key_grad, value_grad = lax.map(per_head, (query_heads, grad_heads, key_heads, value_heads))
    grad_queries = query_grad.transpose(2, 0, 1, 3).reshape(key_count, HEADS * HEAD_DIM).astype(jnp.bfloat16)
    grad_keys = key_grad.transpose(1, 0, 2).reshape(key_count, KV_HEADS * HEAD_DIM).astype(jnp.bfloat16)
    grad_values = value_grad.transpose(1, 0, 2).reshape(key_count, KV_HEADS * HEAD_DIM).astype(jnp.bfloat16)
    return (grad_queries, grad_keys, grad_values)

def reference(queries_cross, outputs_grad, keys_shared, values_shared, stripe_order, segments, norm_input, norm_gain, weight_key, weight_value, upstream, weight_out, queries_window, keys_window, values_window):
    grad_cross, banded_kgrad, banded_vgrad = cross_section(queries_cross, outputs_grad, keys_shared, values_shared, stripe_order, segments)
    inverse = inverse_of(stripe_order)
    key_grad = banded_kgrad[inverse]
    value_grad = banded_vgrad[inverse]
    normed_grad = jnp.dot(key_grad, weight_key.T, preferred_element_type=jnp.float32) + jnp.dot(value_grad, weight_value.T, preferred_element_type=jnp.float32)
    inputs = norm_input.astype(jnp.float32)
    scaling = lax.rsqrt(lax.optimization_barrier(jnp.mean(inputs * inputs, axis=1, keepdims=True)) + 1e-06)
    gained = normed_grad * norm_gain
    inner = lax.optimization_barrier(jnp.mean(gained * inputs, axis=1, keepdims=True))
    stream = scaling * gained - inputs * scaling ** 3 * inner + upstream.astype(jnp.float32)
    grad_stream = stream.astype(jnp.bfloat16)
    head_grads = jnp.dot(grad_stream, weight_out.T, preferred_element_type=jnp.float32).astype(jnp.bfloat16)
    grad_queries, grad_keys, grad_values = window_section(queries_window, head_grads, keys_window, values_window, segments)
    return (grad_cross, grad_stream, grad_queries, grad_keys, grad_values)
```

```python
import jax
import jax.numpy as jnp
from jax import lax
from jax.sharding import PartitionSpec as P

D = 3072
HEADS = 24
KV_HEADS = 8
HEAD_DIM = 128
WINDOW = 1024
DOCS = 8
QUERY_BLOCKS = 4


def from_behind(value, axis, steps):
    count = lax.axis_size(axis)
    first, last = (max(0, -steps), min(count, count - steps))
    return lax.ppermute(value, axis, [(source, source + steps) for source in range(first, last)])


def segment_of(segments, places):
    levels = jnp.arange(1, DOCS, dtype=jnp.int32)
    starts = jnp.sum((segments[None, :] < levels[:, None]).astype(jnp.int32), axis=1)
    return jnp.sum((places[..., None] >= starts).astype(jnp.int32), axis=-1)


def split_heads(matrix):
    row_count = matrix.shape[0]
    return matrix.reshape(row_count, -1, HEAD_DIM).transpose(1, 0, 2)


def join_heads(tensor):
    heads, row_count, width = tensor.shape
    return tensor.transpose(1, 0, 2).reshape(row_count, heads * width)


def attend_block(queries, out_grads, keys, values, allowed):
    factor = HEAD_DIM ** (-0.5)
    scores = (
        jnp.einsum("hre,ke->hrk", queries, keys, preferred_element_type=jnp.float32) * factor
    )
    scores = jnp.where(allowed[None], scores, -jnp.inf)
    row_peak = jnp.max(scores, axis=2, keepdims=True)
    logsum = row_peak + jnp.log(jnp.sum(jnp.exp(scores - row_peak), axis=2, keepdims=True))
    weights = jnp.exp(scores - logsum)
    weights_low = weights.astype(jnp.bfloat16)
    output = jnp.einsum("hrk,ke->hre", weights_low, values, preferred_element_type=jnp.float32)
    row_inner = jnp.sum(out_grads.astype(jnp.float32) * output, axis=2, keepdims=True)
    weight_grads = jnp.einsum(
        "hre,ke->hrk", out_grads, values, preferred_element_type=jnp.float32
    )
    score_grads = (weights * (weight_grads - row_inner)).astype(jnp.bfloat16)
    query_grad = (
        jnp.einsum("hrk,ke->hre", score_grads, keys, preferred_element_type=jnp.float32) * factor
    )
    key_grad = (
        jnp.einsum("hrk,hre->ke", score_grads, queries, preferred_element_type=jnp.float32)
        * factor
    )
    value_grad = jnp.einsum(
        "hrk,hre->ke", weights_low, out_grads, preferred_element_type=jnp.float32
    )
    return query_grad, key_grad, value_grad


def local(
    queries_cross,
    outputs_grad,
    keys_shared,
    values_shared,
    stripe_order,
    segments,
    norm_input,
    norm_gain,
    weight_key,
    weight_value,
    upstream,
    weight_out,
    queries_window,
    keys_window,
    values_window,
):
    row_count = queries_cross.shape[0]
    total_rows = stripe_order.shape[0]
    key_width = keys_shared.shape[1]
    shard_index = lax.axis_index("ctx")
    shard_count = lax.axis_size("ctx")
    stripe = total_rows // row_count
    first_row = shard_index * row_count

    shared = jnp.concatenate([keys_shared, values_shared], axis=1)
    gathered = lax.all_gather(shared, "ctx", axis=0, tiled=True)
    ordered = (
        gathered.reshape(shard_count, row_count, 2 * key_width)
        .transpose(1, 0, 2)
        .reshape(total_rows, 2 * key_width)
    )
    order_table = stripe_order.reshape(shard_count, row_count)
    key_place = order_table.T.reshape(total_rows)
    key_segment = segment_of(segments, key_place)
    query_place = lax.dynamic_slice_in_dim(stripe_order, first_row, row_count)
    query_segment = segment_of(segments, query_place)
    queries = split_heads(queries_cross)
    out_grads = split_heads(outputs_grad)
    block_rows = row_count // QUERY_BLOCKS
    query_grads = []
    key_total = jnp.zeros((total_rows, key_width), jnp.float32)
    value_total = jnp.zeros((total_rows, key_width), jnp.float32)
    for block in range(QUERY_BLOCKS):
        low = block * block_rows
        reach = (low + block_rows) * stripe
        block_place = query_place[low : low + block_rows]
        block_segment = query_segment[low : low + block_rows]
        allowed = (key_place[None, :reach] <= block_place[:, None]) & (
            key_segment[None, :reach] == block_segment[:, None]
        )
        query_grad, key_grad, value_grad = attend_block(
            queries[:, low : low + block_rows],
            out_grads[:, low : low + block_rows],
            ordered[:reach, :key_width],
            ordered[:reach, key_width:],
            allowed,
        )
        query_grads.append(query_grad)
        pad = ((0, total_rows - reach), (0, 0))
        key_total = key_total + jnp.pad(key_grad, pad)
        value_total = value_total + jnp.pad(value_grad, pad)
    grad_cross = join_heads(jnp.concatenate(query_grads, axis=1)).astype(jnp.bfloat16)

    partial = jnp.concatenate([key_total, value_total], axis=1)
    summed = lax.psum_scatter(partial, "ctx", scatter_dimension=0, tiled=True).astype(
        jnp.bfloat16
    )
    per_shard = row_count // stripe
    held_place = (
        lax.dynamic_slice_in_dim(order_table, shard_index * per_shard, per_shard, axis=1)
        .T.reshape(row_count)
    )
    local_place = held_place - first_row
    placement = (
        local_place[None, :] == jnp.arange(row_count, dtype=jnp.int32)[:, None]
    ).astype(jnp.bfloat16)
    shared_grad = jnp.dot(placement, summed, preferred_element_type=jnp.float32).astype(
        jnp.bfloat16
    )

    contract = (((1,), (1,)), ((), ()))
    normed_part = lax.dot_general(
        shared_grad[:, :key_width], weight_key, contract, preferred_element_type=jnp.float32
    )
    normed_part = normed_part + lax.dot_general(
        shared_grad[:, key_width:], weight_value, contract, preferred_element_type=jnp.float32
    )
    normed_cols = lax.psum_scatter(normed_part, "head", scatter_dimension=1, tiled=True)
    column_count = norm_input.shape[1]
    gain_cols = lax.dynamic_slice_in_dim(
        norm_gain, lax.axis_index("head") * column_count, column_count
    )
    inputs = norm_input.astype(jnp.float32)
    gained = normed_cols * gain_cols[None, :]
    square_sum, inner_sum = lax.psum(
        (jnp.sum(inputs * inputs, axis=1), jnp.sum(gained * inputs, axis=1)), "head"
    )
    scaling = lax.rsqrt(square_sum / D + 1e-06)[:, None]
    stream = (
        scaling * gained
        - inputs * scaling**3 * (inner_sum / D)[:, None]
        + upstream.astype(jnp.float32)
    )
    grad_stream = stream.astype(jnp.bfloat16)
    stream_full = lax.all_gather(grad_stream, "head", axis=1, tiled=True)
    head_grads = lax.dot_general(
        stream_full, weight_out, contract, preferred_element_type=jnp.float32
    ).astype(jnp.bfloat16)

    reach_count = WINDOW // row_count
    own_window = jnp.concatenate([keys_window, values_window], axis=1)
    pieces = [from_behind(own_window, "ctx", distance) for distance in range(reach_count, 0, -1)]
    window_all = jnp.concatenate(pieces + [own_window], axis=0)
    own_place = first_row + jnp.arange(row_count, dtype=jnp.int32)
    window_place = first_row - WINDOW + jnp.arange(WINDOW + row_count, dtype=jnp.int32)
    padded = jnp.concatenate([jnp.full((WINDOW,), -1, jnp.int32), segments])
    window_segment = lax.dynamic_slice_in_dim(padded, first_row, WINDOW + row_count)
    own_segment = lax.dynamic_slice_in_dim(segments, first_row, row_count)
    allowed = (
        (window_place[None, :] <= own_place[:, None])
        & (window_place[None, :] > own_place[:, None] - WINDOW)
        & (window_segment[None, :] == own_segment[:, None])
    )
    window_qgrad, window_kgrad, window_vgrad = attend_block(
        split_heads(queries_window),
        split_heads(head_grads),
        window_all[:, :key_width],
        window_all[:, key_width:],
        allowed,
    )
    grad_queries = join_heads(window_qgrad).astype(jnp.bfloat16)
    window_part = jnp.concatenate([window_kgrad, window_vgrad], axis=1)
    collected = window_part[WINDOW:]
    for distance in range(1, reach_count + 1):
        lower_row = (reach_count - distance) * row_count
        collected = collected + from_behind(
            window_part[lower_row : lower_row + row_count], "ctx", -distance
        )
    grad_keys = collected[:, :key_width].astype(jnp.bfloat16)
    grad_values = collected[:, key_width:].astype(jnp.bfloat16)
    return (grad_cross, grad_stream, grad_queries, grad_keys, grad_values)


def solution(mesh):
    in_specs = (
        P("ctx", "head"),
        P("ctx", "head"),
        P("ctx", "head"),
        P("ctx", "head"),
        P(),
        P(),
        P("ctx", "head"),
        P(),
        P(None, "head"),
        P(None, "head"),
        P("ctx", "head"),
        P("head", None),
        P("ctx", "head"),
        P("ctx", "head"),
        P("ctx", "head"),
    )
    out_specs = (
        P("ctx", "head"),
        P("ctx", "head"),
        P("ctx", "head"),
        P("ctx", "head"),
        P("ctx", "head"),
    )
    return jax.shard_map(local, mesh=mesh, in_specs=in_specs, out_specs=out_specs, check_vma=False)
```

```python
import jax
import jax.numpy as jnp
from jax import lax
from jax.sharding import PartitionSpec as P

D = 3072
HEADS = 24
KV_HEADS = 8
HEAD_DIM = 128
WINDOW = 1024
DOCS = 8
QUERY_BLOCKS = 4


def from_behind(value, axis, steps):
    count = lax.axis_size(axis)
    first, last = (max(0, -steps), min(count, count - steps))
    return lax.ppermute(value, axis, [(source, source + steps) for source in range(first, last)])


def segment_of(segments, places):
    levels = jnp.arange(1, DOCS, dtype=jnp.int32)
    starts = jnp.sum((segments[None, :] < levels[:, None]).astype(jnp.int32), axis=1)
    return jnp.sum((places[..., None] >= starts).astype(jnp.int32), axis=-1)


def split_heads(matrix):
    row_count = matrix.shape[0]
    return matrix.reshape(row_count, -1, HEAD_DIM).transpose(1, 0, 2)


def join_heads(tensor):
    heads, row_count, width = tensor.shape
    return tensor.transpose(1, 0, 2).reshape(row_count, heads * width)


def attend_block(queries, out_grads, keys, values, allowed):
    factor = HEAD_DIM ** (-0.5)
    scores = (
        jnp.einsum("hre,ke->hrk", queries, keys, preferred_element_type=jnp.float32) * factor
    )
    scores = jnp.where(allowed[None], scores, -jnp.inf)
    row_peak = jnp.max(scores, axis=2, keepdims=True)
    logsum = row_peak + jnp.log(jnp.sum(jnp.exp(scores - row_peak), axis=2, keepdims=True))
    weights = jnp.exp(scores - logsum)
    weights_low = weights.astype(jnp.bfloat16)
    output = jnp.einsum("hrk,ke->hre", weights_low, values, preferred_element_type=jnp.float32)
    row_inner = jnp.sum(out_grads.astype(jnp.float32) * output, axis=2, keepdims=True)
    weight_grads = jnp.einsum(
        "hre,ke->hrk", out_grads, values, preferred_element_type=jnp.float32
    )
    score_grads = (weights * (weight_grads - row_inner)).astype(jnp.bfloat16)
    query_grad = (
        jnp.einsum("hrk,ke->hre", score_grads, keys, preferred_element_type=jnp.float32) * factor
    )
    key_grad = (
        jnp.einsum("hrk,hre->ke", score_grads, queries, preferred_element_type=jnp.float32)
        * factor
    )
    value_grad = jnp.einsum(
        "hrk,hre->ke", weights_low, out_grads, preferred_element_type=jnp.float32
    )
    return query_grad, key_grad, value_grad


def local(
    queries_cross,
    outputs_grad,
    keys_shared,
    values_shared,
    stripe_order,
    segments,
    norm_input,
    norm_gain,
    weight_key,
    weight_value,
    upstream,
    weight_out,
    queries_window,
    keys_window,
    values_window,
):
    row_count = queries_cross.shape[0]
    total_rows = stripe_order.shape[0]
    key_width = keys_shared.shape[1]
    shard_index = lax.axis_index("ctx")
    shard_count = lax.axis_size("ctx")
    stripe = total_rows // row_count
    first_row = shard_index * row_count

    shared = jnp.concatenate([keys_shared, values_shared], axis=1)
    gathered = lax.all_gather(shared, "ctx", axis=0, tiled=True)
    ordered = (
        gathered.reshape(shard_count, row_count, 2 * key_width)
        .transpose(1, 0, 2)
        .reshape(total_rows, 2 * key_width)
    )
    order_table = stripe_order.reshape(shard_count, row_count)
    key_place = order_table.T.reshape(total_rows)
    key_segment = segment_of(segments, key_place)
    query_place = lax.dynamic_slice_in_dim(stripe_order, first_row, row_count)
    query_segment = segment_of(segments, query_place)
    queries = split_heads(queries_cross)
    out_grads = split_heads(outputs_grad)
    block_rows = row_count // QUERY_BLOCKS
    query_grads = []
    key_total = jnp.zeros((total_rows, key_width), jnp.float32)
    value_total = jnp.zeros((total_rows, key_width), jnp.float32)
    for block in range(QUERY_BLOCKS):
        low = block * block_rows
        reach = (low + block_rows) * stripe
        block_place = query_place[low : low + block_rows]
        block_segment = query_segment[low : low + block_rows]
        allowed = (key_place[None, :reach] <= block_place[:, None]) & (
            key_segment[None, :reach] == block_segment[:, None]
        )
        query_grad, key_grad, value_grad = attend_block(
            queries[:, low : low + block_rows],
            out_grads[:, low : low + block_rows],
            ordered[:reach, :key_width],
            ordered[:reach, key_width:],
            allowed,
        )
        query_grads.append(query_grad)
        pad = ((0, total_rows - reach), (0, 0))
        key_total = key_total + jnp.pad(key_grad, pad)
        value_total = value_total + jnp.pad(value_grad, pad)
    grad_cross = join_heads(jnp.concatenate(query_grads, axis=1)).astype(jnp.bfloat16)

    partial = jnp.concatenate([key_total, value_total], axis=1).astype(jnp.bfloat16)
    arrived = lax.all_to_all(
        partial.reshape(shard_count, row_count, 2 * key_width),
        "ctx",
        split_axis=0,
        concat_axis=0,
        tiled=True,
    )
    summed = jnp.sum(arrived.astype(jnp.float32), axis=0).astype(jnp.bfloat16)
    per_shard = row_count // stripe
    held_place = (
        lax.dynamic_slice_in_dim(order_table, shard_index * per_shard, per_shard, axis=1)
        .T.reshape(row_count)
    )
    local_place = held_place - first_row
    placement = (
        local_place[None, :] == jnp.arange(row_count, dtype=jnp.int32)[:, None]
    ).astype(jnp.bfloat16)
    shared_grad = jnp.dot(placement, summed, preferred_element_type=jnp.float32).astype(
        jnp.bfloat16
    )

    contract = (((1,), (1,)), ((), ()))
    normed_part = lax.dot_general(
        shared_grad[:, :key_width], weight_key, contract, preferred_element_type=jnp.float32
    )
    normed_part = normed_part + lax.dot_general(
        shared_grad[:, key_width:], weight_value, contract, preferred_element_type=jnp.float32
    )
    normed_cols = lax.psum_scatter(normed_part, "head", scatter_dimension=1, tiled=True)
    column_count = norm_input.shape[1]
    gain_cols = lax.dynamic_slice_in_dim(
        norm_gain, lax.axis_index("head") * column_count, column_count
    )
    inputs = norm_input.astype(jnp.float32)
    gained = normed_cols * gain_cols[None, :]
    square_sum, inner_sum = lax.psum(
        (jnp.sum(inputs * inputs, axis=1), jnp.sum(gained * inputs, axis=1)), "head"
    )
    scaling = lax.rsqrt(square_sum / D + 1e-06)[:, None]
    stream = (
        scaling * gained
        - inputs * scaling**3 * (inner_sum / D)[:, None]
        + upstream.astype(jnp.float32)
    )
    grad_stream = stream.astype(jnp.bfloat16)
    stream_full = lax.all_gather(grad_stream, "head", axis=1, tiled=True)
    head_grads = lax.dot_general(
        stream_full, weight_out, contract, preferred_element_type=jnp.float32
    ).astype(jnp.bfloat16)

    reach_count = WINDOW // row_count
    own_window = jnp.concatenate([keys_window, values_window], axis=1)
    pieces = [from_behind(own_window, "ctx", distance) for distance in range(reach_count, 0, -1)]
    window_all = jnp.concatenate(pieces + [own_window], axis=0)
    own_place = first_row + jnp.arange(row_count, dtype=jnp.int32)
    window_place = first_row - WINDOW + jnp.arange(WINDOW + row_count, dtype=jnp.int32)
    padded = jnp.concatenate([jnp.full((WINDOW,), -1, jnp.int32), segments])
    window_segment = lax.dynamic_slice_in_dim(padded, first_row, WINDOW + row_count)
    own_segment = lax.dynamic_slice_in_dim(segments, first_row, row_count)
    allowed = (
        (window_place[None, :] <= own_place[:, None])
        & (window_place[None, :] > own_place[:, None] - WINDOW)
        & (window_segment[None, :] == own_segment[:, None])
    )
    window_qgrad, window_kgrad, window_vgrad = attend_block(
        split_heads(queries_window),
        split_heads(head_grads),
        window_all[:, :key_width],
        window_all[:, key_width:],
        allowed,
    )
    grad_queries = join_heads(window_qgrad).astype(jnp.bfloat16)
    window_part = jnp.concatenate([window_kgrad, window_vgrad], axis=1)
    collected = window_part[WINDOW:]
    for distance in range(1, reach_count + 1):
        lower_row = (reach_count - distance) * row_count
        collected = collected + from_behind(
            window_part[lower_row : lower_row + row_count], "ctx", -distance
        )
    grad_keys = collected[:, :key_width].astype(jnp.bfloat16)
    grad_values = collected[:, key_width:].astype(jnp.bfloat16)
    return (grad_cross, grad_stream, grad_queries, grad_keys, grad_values)


def solution(mesh):
    in_specs = (
        P("ctx", "head"),
        P("ctx", "head"),
        P("ctx", "head"),
        P("ctx", "head"),
        P(),
        P(),
        P("ctx", "head"),
        P(),
        P(None, "head"),
        P(None, "head"),
        P("ctx", "head"),
        P("head", None),
        P("ctx", "head"),
        P("ctx", "head"),
        P("ctx", "head"),
    )
    out_specs = (
        P("ctx", "head"),
        P("ctx", "head"),
        P("ctx", "head"),
        P("ctx", "head"),
        P("ctx", "head"),
    )
    return jax.shard_map(local, mesh=mesh, in_specs=in_specs, out_specs=out_specs, check_vma=False)
```

```python
import jax
import jax.numpy as jnp
from jax import lax
from jax.sharding import PartitionSpec as P

D = 3072
HEADS = 24
KV_HEADS = 8
HEAD_DIM = 128
WINDOW = 1024
DOCS = 8
QUERY_BLOCKS = 4
CTX = ("z", "yh", "core")
HEAD = ("yl", "x")


def from_behind(value, axis, steps):
    count = lax.axis_size(axis)
    first, last = (max(0, -steps), min(count, count - steps))
    return lax.ppermute(value, axis, [(source, source + steps) for source in range(first, last)])


def segment_of(segments, places):
    levels = jnp.arange(1, DOCS, dtype=jnp.int32)
    starts = jnp.sum((segments[None, :] < levels[:, None]).astype(jnp.int32), axis=1)
    return jnp.sum((places[..., None] >= starts).astype(jnp.int32), axis=-1)


def split_heads(matrix):
    row_count = matrix.shape[0]
    return matrix.reshape(row_count, -1, HEAD_DIM).transpose(1, 0, 2)


def join_heads(tensor):
    heads, row_count, width = tensor.shape
    return tensor.transpose(1, 0, 2).reshape(row_count, heads * width)


def attend_block(queries, out_grads, keys, values, allowed):
    factor = HEAD_DIM ** (-0.5)
    scores = (
        jnp.einsum("hre,ke->hrk", queries, keys, preferred_element_type=jnp.float32) * factor
    )
    scores = jnp.where(allowed[None], scores, -jnp.inf)
    row_peak = jnp.max(scores, axis=2, keepdims=True)
    logsum = row_peak + jnp.log(jnp.sum(jnp.exp(scores - row_peak), axis=2, keepdims=True))
    weights = jnp.exp(scores - logsum)
    weights_low = weights.astype(jnp.bfloat16)
    output = jnp.einsum("hrk,ke->hre", weights_low, values, preferred_element_type=jnp.float32)
    row_inner = jnp.sum(out_grads.astype(jnp.float32) * output, axis=2, keepdims=True)
    weight_grads = jnp.einsum(
        "hre,ke->hrk", out_grads, values, preferred_element_type=jnp.float32
    )
    score_grads = (weights * (weight_grads - row_inner)).astype(jnp.bfloat16)
    query_grad = (
        jnp.einsum("hrk,ke->hre", score_grads, keys, preferred_element_type=jnp.float32) * factor
    )
    key_grad = (
        jnp.einsum("hrk,hre->ke", score_grads, queries, preferred_element_type=jnp.float32)
        * factor
    )
    value_grad = jnp.einsum(
        "hrk,hre->ke", weights_low, out_grads, preferred_element_type=jnp.float32
    )
    return query_grad, key_grad, value_grad


def local(
    queries_cross,
    outputs_grad,
    keys_shared,
    values_shared,
    stripe_order,
    segments,
    norm_input,
    norm_gain,
    weight_key,
    weight_value,
    upstream,
    weight_out,
    queries_window,
    keys_window,
    values_window,
):
    row_count = queries_cross.shape[0]
    total_rows = stripe_order.shape[0]
    key_width = keys_shared.shape[1]
    shard_index = lax.axis_index(CTX)
    shard_count = lax.axis_size(CTX)
    stripe = total_rows // row_count
    first_row = shard_index * row_count

    shared = jnp.concatenate([keys_shared, values_shared], axis=1)
    gathered = shared
    for axis in reversed(CTX):
        gathered = lax.all_gather(gathered, axis, axis=0, tiled=True)
    ordered = (
        gathered.reshape(shard_count, row_count, 2 * key_width)
        .transpose(1, 0, 2)
        .reshape(total_rows, 2 * key_width)
    )
    order_table = stripe_order.reshape(shard_count, row_count)
    key_place = order_table.T.reshape(total_rows)
    key_segment = segment_of(segments, key_place)
    query_place = lax.dynamic_slice_in_dim(stripe_order, first_row, row_count)
    query_segment = segment_of(segments, query_place)
    queries = split_heads(queries_cross)
    out_grads = split_heads(outputs_grad)
    block_rows = row_count // QUERY_BLOCKS
    query_grads = []
    key_total = jnp.zeros((total_rows, key_width), jnp.float32)
    value_total = jnp.zeros((total_rows, key_width), jnp.float32)
    for block in range(QUERY_BLOCKS):
        low = block * block_rows
        reach = (low + block_rows) * stripe
        block_place = query_place[low : low + block_rows]
        block_segment = query_segment[low : low + block_rows]
        allowed = (key_place[None, :reach] <= block_place[:, None]) & (
            key_segment[None, :reach] == block_segment[:, None]
        )
        query_grad, key_grad, value_grad = attend_block(
            queries[:, low : low + block_rows],
            out_grads[:, low : low + block_rows],
            ordered[:reach, :key_width],
            ordered[:reach, key_width:],
            allowed,
        )
        query_grads.append(query_grad)
        pad = ((0, total_rows - reach), (0, 0))
        key_total = key_total + jnp.pad(key_grad, pad)
        value_total = value_total + jnp.pad(value_grad, pad)
    grad_cross = join_heads(jnp.concatenate(query_grads, axis=1)).astype(jnp.bfloat16)

    partial = jnp.concatenate([key_total, value_total], axis=1).astype(jnp.bfloat16)
    sizes = tuple(lax.axis_size(axis) for axis in CTX)
    summed = partial.reshape(sizes + (row_count, 2 * key_width))
    for place in reversed(range(len(CTX))):
        arrived = lax.all_to_all(summed, CTX[place], split_axis=place, concat_axis=place, tiled=True)
        summed = jnp.sum(arrived.astype(jnp.float32), axis=place).astype(jnp.bfloat16)
    per_shard = row_count // stripe
    held_place = (
        lax.dynamic_slice_in_dim(order_table, shard_index * per_shard, per_shard, axis=1)
        .T.reshape(row_count)
    )
    local_place = held_place - first_row
    placement = (
        local_place[None, :] == jnp.arange(row_count, dtype=jnp.int32)[:, None]
    ).astype(jnp.bfloat16)
    shared_grad = jnp.dot(placement, summed, preferred_element_type=jnp.float32).astype(
        jnp.bfloat16
    )

    contract = (((1,), (1,)), ((), ()))
    normed_part = lax.dot_general(
        shared_grad[:, :key_width], weight_key, contract, preferred_element_type=jnp.float32
    )
    normed_part = normed_part + lax.dot_general(
        shared_grad[:, key_width:], weight_value, contract, preferred_element_type=jnp.float32
    )
    normed_cols = normed_part
    for axis in HEAD:
        normed_cols = lax.psum_scatter(normed_cols, axis, scatter_dimension=1, tiled=True)
    column_count = norm_input.shape[1]
    gain_cols = lax.dynamic_slice_in_dim(
        norm_gain, lax.axis_index(HEAD) * column_count, column_count
    )
    inputs = norm_input.astype(jnp.float32)
    gained = normed_cols * gain_cols[None, :]
    square_sum, inner_sum = lax.psum(
        (jnp.sum(inputs * inputs, axis=1), jnp.sum(gained * inputs, axis=1)), HEAD
    )
    scaling = lax.rsqrt(square_sum / D + 1e-06)[:, None]
    stream = (
        scaling * gained
        - inputs * scaling**3 * (inner_sum / D)[:, None]
        + upstream.astype(jnp.float32)
    )
    grad_stream = stream.astype(jnp.bfloat16)
    stream_full = grad_stream
    for axis in reversed(HEAD):
        stream_full = lax.all_gather(stream_full, axis, axis=1, tiled=True)
    head_grads = lax.dot_general(
        stream_full, weight_out, contract, preferred_element_type=jnp.float32
    ).astype(jnp.bfloat16)

    reach_count = WINDOW // row_count
    own_window = jnp.concatenate([keys_window, values_window], axis=1)
    pieces = [from_behind(own_window, CTX, distance) for distance in range(reach_count, 0, -1)]
    window_all = jnp.concatenate(pieces + [own_window], axis=0)
    own_place = first_row + jnp.arange(row_count, dtype=jnp.int32)
    window_place = first_row - WINDOW + jnp.arange(WINDOW + row_count, dtype=jnp.int32)
    padded = jnp.concatenate([jnp.full((WINDOW,), -1, jnp.int32), segments])
    window_segment = lax.dynamic_slice_in_dim(padded, first_row, WINDOW + row_count)
    own_segment = lax.dynamic_slice_in_dim(segments, first_row, row_count)
    allowed = (
        (window_place[None, :] <= own_place[:, None])
        & (window_place[None, :] > own_place[:, None] - WINDOW)
        & (window_segment[None, :] == own_segment[:, None])
    )
    window_qgrad, window_kgrad, window_vgrad = attend_block(
        split_heads(queries_window),
        split_heads(head_grads),
        window_all[:, :key_width],
        window_all[:, key_width:],
        allowed,
    )
    grad_queries = join_heads(window_qgrad).astype(jnp.bfloat16)
    window_part = jnp.concatenate([window_kgrad, window_vgrad], axis=1)
    collected = window_part[WINDOW:]
    for distance in range(1, reach_count + 1):
        lower_row = (reach_count - distance) * row_count
        collected = collected + from_behind(
            window_part[lower_row : lower_row + row_count], CTX, -distance
        )
    grad_keys = collected[:, :key_width].astype(jnp.bfloat16)
    grad_values = collected[:, key_width:].astype(jnp.bfloat16)
    return (grad_cross, grad_stream, grad_queries, grad_keys, grad_values)


def solution(mesh):
    ctx_parts = (mesh.shape["ctx"] // 8, 4, 2)
    head_parts = (2, mesh.shape["head"] // 2)
    parts = jax.sharding.Mesh(
        mesh.devices.reshape(ctx_parts + head_parts), CTX + HEAD
    )
    rows = P(CTX, HEAD)
    in_specs = (
        rows,
        rows,
        rows,
        rows,
        P(),
        P(),
        rows,
        P(),
        P(None, HEAD),
        P(None, HEAD),
        rows,
        P(HEAD, None),
        rows,
        rows,
        rows,
    )
    out_specs = (rows, rows, rows, rows, rows)
    return jax.shard_map(local, mesh=parts, in_specs=in_specs, out_specs=out_specs, check_vma=False)
```

```python
import jax
import jax.numpy as jnp
from jax import lax
from jax.sharding import PartitionSpec as P

D = 3072
HEADS = 24
KV_HEADS = 8
HEAD_DIM = 128
WINDOW = 1024
DOCS = 8
QUERY_BLOCKS = 4
CTX = ("z", "yh", "core")
HEAD = ("yl", "x")


def from_behind(value, axis, steps):
    count = lax.axis_size(axis)
    first, last = (max(0, -steps), min(count, count - steps))
    return lax.ppermute(value, axis, [(source, source + steps) for source in range(first, last)])


def segment_of(segments, places):
    levels = jnp.arange(1, DOCS, dtype=jnp.int32)
    starts = jnp.sum((segments[None, :] < levels[:, None]).astype(jnp.int32), axis=1)
    return jnp.sum((places[..., None] >= starts).astype(jnp.int32), axis=-1)


def split_heads(matrix):
    row_count = matrix.shape[0]
    return matrix.reshape(row_count, -1, HEAD_DIM).transpose(1, 0, 2)


def join_heads(tensor):
    heads, row_count, width = tensor.shape
    return tensor.transpose(1, 0, 2).reshape(row_count, heads * width)


def attend_block(queries, out_grads, keys, values, allowed):
    factor = HEAD_DIM ** (-0.5)
    scores = (
        jnp.einsum("hre,ke->hrk", queries, keys, preferred_element_type=jnp.float32) * factor
    )
    scores = jnp.where(allowed[None], scores, -jnp.inf)
    row_peak = jnp.max(scores, axis=2, keepdims=True)
    logsum = row_peak + jnp.log(jnp.sum(jnp.exp(scores - row_peak), axis=2, keepdims=True))
    weights = jnp.exp(scores - logsum)
    weights_low = weights.astype(jnp.bfloat16)
    output = jnp.einsum("hrk,ke->hre", weights_low, values, preferred_element_type=jnp.float32)
    row_inner = jnp.sum(out_grads.astype(jnp.float32) * output, axis=2, keepdims=True)
    weight_grads = jnp.einsum(
        "hre,ke->hrk", out_grads, values, preferred_element_type=jnp.float32
    )
    score_grads = (weights * (weight_grads - row_inner)).astype(jnp.bfloat16)
    query_grad = (
        jnp.einsum("hrk,ke->hre", score_grads, keys, preferred_element_type=jnp.float32) * factor
    )
    key_grad = (
        jnp.einsum("hrk,hre->ke", score_grads, queries, preferred_element_type=jnp.float32)
        * factor
    )
    value_grad = jnp.einsum(
        "hrk,hre->ke", weights_low, out_grads, preferred_element_type=jnp.float32
    )
    return query_grad, key_grad, value_grad


def local(
    queries_cross,
    outputs_grad,
    keys_shared,
    values_shared,
    stripe_order,
    segments,
    norm_input,
    norm_gain,
    weight_key,
    weight_value,
    upstream,
    weight_out,
    queries_window,
    keys_window,
    values_window,
):
    row_count = queries_cross.shape[0]
    total_rows = stripe_order.shape[0]
    key_width = keys_shared.shape[1]
    shard_index = lax.axis_index(CTX)
    shard_count = lax.axis_size(CTX)
    stripe = total_rows // row_count
    first_row = shard_index * row_count

    shared = jnp.concatenate([keys_shared, values_shared], axis=1)
    gathered = shared
    for axis in reversed(CTX):
        gathered = lax.all_gather(gathered, axis, axis=0, tiled=True)
    ordered = (
        gathered.reshape(shard_count, row_count, 2 * key_width)
        .transpose(1, 0, 2)
        .reshape(total_rows, 2 * key_width)
    )
    order_table = stripe_order.reshape(shard_count, row_count)
    key_place = order_table.T.reshape(total_rows)
    key_segment = segment_of(segments, key_place)
    query_place = lax.dynamic_slice_in_dim(stripe_order, first_row, row_count)
    query_segment = segment_of(segments, query_place)
    queries = split_heads(queries_cross)
    out_grads = split_heads(outputs_grad)
    block_rows = row_count // QUERY_BLOCKS
    query_grads = []
    key_total = jnp.zeros((total_rows, key_width), jnp.float32)
    value_total = jnp.zeros((total_rows, key_width), jnp.float32)
    for block in range(QUERY_BLOCKS):
        low = block * block_rows
        reach = (low + block_rows) * stripe
        block_place = query_place[low : low + block_rows]
        block_segment = query_segment[low : low + block_rows]
        allowed = (key_place[None, :reach] <= block_place[:, None]) & (
            key_segment[None, :reach] == block_segment[:, None]
        )
        query_grad, key_grad, value_grad = attend_block(
            queries[:, low : low + block_rows],
            out_grads[:, low : low + block_rows],
            ordered[:reach, :key_width],
            ordered[:reach, key_width:],
            allowed,
        )
        query_grads.append(query_grad)
        pad = ((0, total_rows - reach), (0, 0))
        key_total = key_total + jnp.pad(key_grad, pad)
        value_total = value_total + jnp.pad(value_grad, pad)
    grad_cross = join_heads(jnp.concatenate(query_grads, axis=1)).astype(jnp.bfloat16)

    partial = jnp.concatenate([key_total, value_total], axis=1).astype(jnp.bfloat16)
    sizes = tuple(lax.axis_size(axis) for axis in CTX)
    summed = partial.reshape(sizes + (row_count, 2 * key_width))
    for place in reversed(range(len(CTX))):
        arrived = lax.all_to_all(summed, CTX[place], split_axis=place, concat_axis=place, tiled=True)
        summed = jnp.sum(arrived.astype(jnp.float32), axis=place).astype(jnp.bfloat16)
    per_shard = row_count // stripe
    held_place = (
        lax.dynamic_slice_in_dim(order_table, shard_index * per_shard, per_shard, axis=1)
        .T.reshape(row_count)
    )
    local_place = held_place - first_row
    placement = (
        local_place[None, :] == jnp.arange(row_count, dtype=jnp.int32)[:, None]
    ).astype(jnp.bfloat16)
    shared_grad = jnp.dot(placement, summed, preferred_element_type=jnp.float32).astype(
        jnp.bfloat16
    )

    contract = (((1,), (1,)), ((), ()))
    normed_part = lax.dot_general(
        shared_grad[:, :key_width], weight_key, contract, preferred_element_type=jnp.float32
    )
    normed_part = normed_part + lax.dot_general(
        shared_grad[:, key_width:], weight_value, contract, preferred_element_type=jnp.float32
    )
    column_count = norm_input.shape[1]
    inputs_full = norm_input
    for axis in reversed(HEAD):
        inputs_full = lax.all_gather(inputs_full, axis, axis=1, tiled=True)
    inputs_full = inputs_full.astype(jnp.float32)
    square_sum = jnp.sum(inputs_full * inputs_full, axis=1)
    inner_part = jnp.sum(normed_part * norm_gain[None, :] * inputs_full, axis=1)
    head_count = normed_part.shape[1] // column_count
    extra = jnp.tile(jnp.pad(inner_part, (0, column_count - row_count)), head_count)
    reduced = jnp.concatenate([normed_part, extra[None, :]], axis=0)
    for axis in HEAD:
        reduced = lax.psum_scatter(reduced, axis, scatter_dimension=1, tiled=True)
    normed_cols = reduced[:row_count]
    inner_sum = reduced[row_count, :row_count]
    gain_cols = lax.dynamic_slice_in_dim(
        norm_gain, lax.axis_index(HEAD) * column_count, column_count
    )
    inputs = norm_input.astype(jnp.float32)
    gained = normed_cols * gain_cols[None, :]
    scaling = lax.rsqrt(square_sum / D + 1e-06)[:, None]
    stream = (
        scaling * gained
        - inputs * scaling**3 * (inner_sum / D)[:, None]
        + upstream.astype(jnp.float32)
    )
    grad_stream = stream.astype(jnp.bfloat16)
    stream_full = grad_stream
    for axis in reversed(HEAD):
        stream_full = lax.all_gather(stream_full, axis, axis=1, tiled=True)
    head_grads = lax.dot_general(
        stream_full, weight_out, contract, preferred_element_type=jnp.float32
    ).astype(jnp.bfloat16)

    reach_count = WINDOW // row_count
    own_window = jnp.concatenate([keys_window, values_window], axis=1)
    block = own_window
    for axis in reversed(CTX[1:]):
        block = lax.all_gather(block, axis, axis=0, tiled=True)
    earlier = from_behind(block, CTX[0], 1)
    frame = jnp.concatenate([earlier, block], axis=0)
    in_block = shard_index % (block.shape[0] // row_count)
    window_all = lax.dynamic_slice_in_dim(frame, in_block * row_count, WINDOW + row_count)
    own_place = first_row + jnp.arange(row_count, dtype=jnp.int32)
    window_place = first_row - WINDOW + jnp.arange(WINDOW + row_count, dtype=jnp.int32)
    padded = jnp.concatenate([jnp.full((WINDOW,), -1, jnp.int32), segments])
    window_segment = lax.dynamic_slice_in_dim(padded, first_row, WINDOW + row_count)
    own_segment = lax.dynamic_slice_in_dim(segments, first_row, row_count)
    allowed = (
        (window_place[None, :] <= own_place[:, None])
        & (window_place[None, :] > own_place[:, None] - WINDOW)
        & (window_segment[None, :] == own_segment[:, None])
    )
    window_qgrad, window_kgrad, window_vgrad = attend_block(
        split_heads(queries_window),
        split_heads(head_grads),
        window_all[:, :key_width],
        window_all[:, key_width:],
        allowed,
    )
    grad_queries = join_heads(window_qgrad).astype(jnp.bfloat16)
    window_part = jnp.concatenate([window_kgrad, window_vgrad], axis=1)
    collected = window_part[WINDOW:]
    for distance in range(1, reach_count + 1):
        lower_row = (reach_count - distance) * row_count
        collected = collected + from_behind(
            window_part[lower_row : lower_row + row_count], CTX, -distance
        )
    grad_keys = collected[:, :key_width].astype(jnp.bfloat16)
    grad_values = collected[:, key_width:].astype(jnp.bfloat16)
    return (grad_cross, grad_stream, grad_queries, grad_keys, grad_values)


def solution(mesh):
    ctx_parts = (mesh.shape["ctx"] // 8, 4, 2)
    head_parts = (2, mesh.shape["head"] // 2)
    parts = jax.sharding.Mesh(
        mesh.devices.reshape(ctx_parts + head_parts), CTX + HEAD
    )
    rows = P(CTX, HEAD)
    in_specs = (
        rows,
        rows,
        rows,
        rows,
        P(),
        P(),
        rows,
        P(),
        P(None, HEAD),
        P(None, HEAD),
        rows,
        P(HEAD, None),
        rows,
        rows,
        rows,
    )
    out_specs = (rows, rows, rows, rows, rows)
    return jax.shard_map(local, mesh=parts, in_specs=in_specs, out_specs=out_specs, check_vma=False)
```

```python
import jax
import jax.numpy as jnp
from jax import lax
from jax.sharding import PartitionSpec as P

D = 3072
HEADS = 24
KV_HEADS = 8
HEAD_DIM = 128
WINDOW = 1024
DOCS = 8
QUERY_BLOCKS = 4
CTX = ("z", "yh", "core")
HEAD = ("yl", "x")


def from_behind(value, axis, steps):
    count = lax.axis_size(axis)
    first, last = (max(0, -steps), min(count, count - steps))
    return lax.ppermute(value, axis, [(source, source + steps) for source in range(first, last)])


def segment_of(segments, places):
    levels = jnp.arange(1, DOCS, dtype=jnp.int32)
    starts = jnp.sum((segments[None, :] < levels[:, None]).astype(jnp.int32), axis=1)
    return jnp.sum((places[..., None] >= starts).astype(jnp.int32), axis=-1)


def split_heads(matrix):
    row_count = matrix.shape[0]
    return matrix.reshape(row_count, -1, HEAD_DIM).transpose(1, 0, 2)


def join_heads(tensor):
    heads, row_count, width = tensor.shape
    return tensor.transpose(1, 0, 2).reshape(row_count, heads * width)


def attend_block(queries, out_grads, keys, values, allowed):
    factor = HEAD_DIM ** (-0.5)
    scores = (
        jnp.einsum("hre,ke->hrk", queries, keys, preferred_element_type=jnp.float32) * factor
    )
    scores = jnp.where(allowed[None], scores, -jnp.inf)
    row_peak = jnp.max(scores, axis=2, keepdims=True)
    logsum = row_peak + jnp.log(jnp.sum(jnp.exp(scores - row_peak), axis=2, keepdims=True))
    weights = jnp.exp(scores - logsum)
    weights_low = weights.astype(jnp.bfloat16)
    output = jnp.einsum("hrk,ke->hre", weights_low, values, preferred_element_type=jnp.float32)
    row_inner = jnp.sum(out_grads.astype(jnp.float32) * output, axis=2, keepdims=True)
    weight_grads = jnp.einsum(
        "hre,ke->hrk", out_grads, values, preferred_element_type=jnp.float32
    )
    score_grads = (weights * (weight_grads - row_inner)).astype(jnp.bfloat16)
    query_grad = (
        jnp.einsum("hrk,ke->hre", score_grads, keys, preferred_element_type=jnp.float32) * factor
    )
    key_grad = (
        jnp.einsum("hrk,hre->ke", score_grads, queries, preferred_element_type=jnp.float32)
        * factor
    )
    value_grad = jnp.einsum(
        "hrk,hre->ke", weights_low, out_grads, preferred_element_type=jnp.float32
    )
    return query_grad, key_grad, value_grad


def local(
    queries_cross,
    outputs_grad,
    keys_shared,
    values_shared,
    stripe_order,
    segments,
    norm_input,
    norm_gain,
    weight_key,
    weight_value,
    upstream,
    weight_out,
    queries_window,
    keys_window,
    values_window,
):
    row_count = queries_cross.shape[0]
    total_rows = stripe_order.shape[0]
    key_width = keys_shared.shape[1]
    shard_index = lax.axis_index(CTX)
    shard_count = lax.axis_size(CTX)
    stripe = total_rows // row_count
    first_row = shard_index * row_count

    shared = jnp.concatenate([keys_shared, values_shared], axis=1)
    gathered = shared
    for axis in reversed(CTX):
        gathered = lax.all_gather(gathered, axis, axis=0, tiled=True)
    column_count = norm_input.shape[1]
    inputs_full = norm_input
    for axis in reversed(HEAD):
        inputs_full = lax.all_gather(inputs_full, axis, axis=1, tiled=True)
    own_window = jnp.concatenate([keys_window, values_window], axis=1)
    window_block = own_window
    for axis in reversed(CTX[1:]):
        window_block = lax.all_gather(window_block, axis, axis=0, tiled=True)
    earlier = from_behind(window_block, CTX[0], 1)
    frame = jnp.concatenate([earlier, window_block], axis=0)
    gathered, inputs_full, frame = lax.optimization_barrier((gathered, inputs_full, frame))
    ordered = (
        gathered.reshape(shard_count, row_count, 2 * key_width)
        .transpose(1, 0, 2)
        .reshape(total_rows, 2 * key_width)
    )
    order_table = stripe_order.reshape(shard_count, row_count)
    key_place = order_table.T.reshape(total_rows)
    key_segment = segment_of(segments, key_place)
    query_place = lax.dynamic_slice_in_dim(stripe_order, first_row, row_count)
    query_segment = segment_of(segments, query_place)
    queries = split_heads(queries_cross)
    out_grads = split_heads(outputs_grad)
    block_rows = row_count // QUERY_BLOCKS
    query_grads = []
    key_total = jnp.zeros((total_rows, key_width), jnp.float32)
    value_total = jnp.zeros((total_rows, key_width), jnp.float32)
    for block in range(QUERY_BLOCKS):
        low = block * block_rows
        reach = (low + block_rows) * stripe
        block_place = query_place[low : low + block_rows]
        block_segment = query_segment[low : low + block_rows]
        allowed = (key_place[None, :reach] <= block_place[:, None]) & (
            key_segment[None, :reach] == block_segment[:, None]
        )
        query_grad, key_grad, value_grad = attend_block(
            queries[:, low : low + block_rows],
            out_grads[:, low : low + block_rows],
            ordered[:reach, :key_width],
            ordered[:reach, key_width:],
            allowed,
        )
        query_grads.append(query_grad)
        pad = ((0, total_rows - reach), (0, 0))
        key_total = key_total + jnp.pad(key_grad, pad)
        value_total = value_total + jnp.pad(value_grad, pad)
    grad_cross = join_heads(jnp.concatenate(query_grads, axis=1)).astype(jnp.bfloat16)

    partial = jnp.concatenate([key_total, value_total], axis=1).astype(jnp.bfloat16)
    sizes = tuple(lax.axis_size(axis) for axis in CTX)
    summed = partial.reshape(sizes + (row_count, 2 * key_width))
    for place in reversed(range(len(CTX))):
        arrived = lax.all_to_all(summed, CTX[place], split_axis=place, concat_axis=place, tiled=True)
        summed = jnp.sum(arrived.astype(jnp.float32), axis=place).astype(jnp.bfloat16)
    per_shard = row_count // stripe
    held_place = (
        lax.dynamic_slice_in_dim(order_table, shard_index * per_shard, per_shard, axis=1)
        .T.reshape(row_count)
    )
    local_place = held_place - first_row
    placement = (
        local_place[None, :] == jnp.arange(row_count, dtype=jnp.int32)[:, None]
    ).astype(jnp.bfloat16)
    shared_grad = jnp.dot(placement, summed, preferred_element_type=jnp.float32).astype(
        jnp.bfloat16
    )

    contract = (((1,), (1,)), ((), ()))
    normed_part = lax.dot_general(
        shared_grad[:, :key_width], weight_key, contract, preferred_element_type=jnp.float32
    )
    normed_part = normed_part + lax.dot_general(
        shared_grad[:, key_width:], weight_value, contract, preferred_element_type=jnp.float32
    )
    inputs_full = inputs_full.astype(jnp.float32)
    square_sum = jnp.sum(inputs_full * inputs_full, axis=1)
    inner_part = jnp.sum(normed_part * norm_gain[None, :] * inputs_full, axis=1)
    head_count = normed_part.shape[1] // column_count
    extra = jnp.tile(jnp.pad(inner_part, (0, column_count - row_count)), head_count)
    reduced = jnp.concatenate([normed_part, extra[None, :]], axis=0)
    for axis in HEAD:
        reduced = lax.psum_scatter(reduced, axis, scatter_dimension=1, tiled=True)
    normed_cols = reduced[:row_count]
    inner_sum = reduced[row_count, :row_count]
    gain_cols = lax.dynamic_slice_in_dim(
        norm_gain, lax.axis_index(HEAD) * column_count, column_count
    )
    inputs = norm_input.astype(jnp.float32)
    gained = normed_cols * gain_cols[None, :]
    scaling = lax.rsqrt(square_sum / D + 1e-06)[:, None]
    stream = (
        scaling * gained
        - inputs * scaling**3 * (inner_sum / D)[:, None]
        + upstream.astype(jnp.float32)
    )
    grad_stream = stream.astype(jnp.bfloat16)
    stream_full = grad_stream
    for axis in reversed(HEAD):
        stream_full = lax.all_gather(stream_full, axis, axis=1, tiled=True)
    head_grads = lax.dot_general(
        stream_full, weight_out, contract, preferred_element_type=jnp.float32
    ).astype(jnp.bfloat16)

    reach_count = WINDOW // row_count
    in_block = shard_index % (window_block.shape[0] // row_count)
    window_all = lax.dynamic_slice_in_dim(frame, in_block * row_count, WINDOW + row_count)
    own_place = first_row + jnp.arange(row_count, dtype=jnp.int32)
    window_place = first_row - WINDOW + jnp.arange(WINDOW + row_count, dtype=jnp.int32)
    padded = jnp.concatenate([jnp.full((WINDOW,), -1, jnp.int32), segments])
    window_segment = lax.dynamic_slice_in_dim(padded, first_row, WINDOW + row_count)
    own_segment = lax.dynamic_slice_in_dim(segments, first_row, row_count)
    allowed = (
        (window_place[None, :] <= own_place[:, None])
        & (window_place[None, :] > own_place[:, None] - WINDOW)
        & (window_segment[None, :] == own_segment[:, None])
    )
    window_qgrad, window_kgrad, window_vgrad = attend_block(
        split_heads(queries_window),
        split_heads(head_grads),
        window_all[:, :key_width],
        window_all[:, key_width:],
        allowed,
    )
    grad_queries = join_heads(window_qgrad).astype(jnp.bfloat16)
    window_part = jnp.concatenate([window_kgrad, window_vgrad], axis=1)
    collected = window_part[WINDOW:]
    for distance in range(1, reach_count + 1):
        lower_row = (reach_count - distance) * row_count
        collected = collected + from_behind(
            window_part[lower_row : lower_row + row_count], CTX, -distance
        )
    grad_keys = collected[:, :key_width].astype(jnp.bfloat16)
    grad_values = collected[:, key_width:].astype(jnp.bfloat16)
    return (grad_cross, grad_stream, grad_queries, grad_keys, grad_values)


def solution(mesh):
    ctx_parts = (mesh.shape["ctx"] // 8, 4, 2)
    head_parts = (2, mesh.shape["head"] // 2)
    parts = jax.sharding.Mesh(
        mesh.devices.reshape(ctx_parts + head_parts), CTX + HEAD
    )
    rows = P(CTX, HEAD)
    in_specs = (
        rows,
        rows,
        rows,
        rows,
        P(),
        P(),
        rows,
        P(),
        P(None, HEAD),
        P(None, HEAD),
        rows,
        P(HEAD, None),
        rows,
        rows,
        rows,
    )
    out_specs = (rows, rows, rows, rows, rows)
    return jax.shard_map(local, mesh=parts, in_specs=in_specs, out_specs=out_specs, check_vma=False)
```

```python
import jax
import jax.numpy as jnp
from jax import lax
from jax.sharding import PartitionSpec as P

D = 3072
HEADS = 24
KV_HEADS = 8
HEAD_DIM = 128
WINDOW = 1024
DOCS = 8
QUERY_BLOCKS = 4
CTX = ("z", "yh", "core")
HEAD = ("yl", "x")


def from_behind(value, axis, steps):
    count = lax.axis_size(axis)
    first, last = (max(0, -steps), min(count, count - steps))
    return lax.ppermute(value, axis, [(source, source + steps) for source in range(first, last)])


def segment_of(segments, places):
    levels = jnp.arange(1, DOCS, dtype=jnp.int32)
    starts = jnp.sum((segments[None, :] < levels[:, None]).astype(jnp.int32), axis=1)
    return jnp.sum((places[..., None] >= starts).astype(jnp.int32), axis=-1)


def split_heads(matrix):
    row_count = matrix.shape[0]
    return matrix.reshape(row_count, -1, HEAD_DIM).transpose(1, 0, 2)


def join_heads(tensor):
    heads, row_count, width = tensor.shape
    return tensor.transpose(1, 0, 2).reshape(row_count, heads * width)


def attend_forward(queries, keys, values, allowed):
    factor = HEAD_DIM ** (-0.5)
    scores = (
        jnp.einsum("hre,ke->hrk", queries, keys, preferred_element_type=jnp.float32) * factor
    )
    scores = jnp.where(allowed[None], scores, -jnp.inf)
    row_peak = jnp.max(scores, axis=2, keepdims=True)
    logsum = row_peak + jnp.log(jnp.sum(jnp.exp(scores - row_peak), axis=2, keepdims=True))
    weights = jnp.exp(scores - logsum)
    weights_low = weights.astype(jnp.bfloat16)
    output = jnp.einsum("hrk,ke->hre", weights_low, values, preferred_element_type=jnp.float32)
    return weights, weights_low, output


def attend_backward(queries, out_grads, keys, values, weights, weights_low, output):
    factor = HEAD_DIM ** (-0.5)
    row_inner = jnp.sum(out_grads.astype(jnp.float32) * output, axis=2, keepdims=True)
    weight_grads = jnp.einsum(
        "hre,ke->hrk", out_grads, values, preferred_element_type=jnp.float32
    )
    score_grads = (weights * (weight_grads - row_inner)).astype(jnp.bfloat16)
    query_grad = (
        jnp.einsum("hrk,ke->hre", score_grads, keys, preferred_element_type=jnp.float32) * factor
    )
    key_grad = (
        jnp.einsum("hrk,hre->ke", score_grads, queries, preferred_element_type=jnp.float32)
        * factor
    )
    value_grad = jnp.einsum(
        "hrk,hre->ke", weights_low, out_grads, preferred_element_type=jnp.float32
    )
    return query_grad, key_grad, value_grad


def attend_block(queries, out_grads, keys, values, allowed):
    weights, weights_low, output = attend_forward(queries, keys, values, allowed)
    return attend_backward(queries, out_grads, keys, values, weights, weights_low, output)


def local(
    queries_cross,
    outputs_grad,
    keys_shared,
    values_shared,
    stripe_order,
    segments,
    norm_input,
    norm_gain,
    weight_key,
    weight_value,
    upstream,
    weight_out,
    queries_window,
    keys_window,
    values_window,
):
    row_count = queries_cross.shape[0]
    total_rows = stripe_order.shape[0]
    key_width = keys_shared.shape[1]
    shard_index = lax.axis_index(CTX)
    shard_count = lax.axis_size(CTX)
    stripe = total_rows // row_count
    first_row = shard_index * row_count

    shared = jnp.concatenate([keys_shared, values_shared], axis=1)
    gathered = shared
    for axis in reversed(CTX):
        gathered = lax.all_gather(gathered, axis, axis=0, tiled=True)
    column_count = norm_input.shape[1]
    inputs_full = norm_input
    for axis in reversed(HEAD):
        inputs_full = lax.all_gather(inputs_full, axis, axis=1, tiled=True)
    own_window = jnp.concatenate([keys_window, values_window], axis=1)
    window_block = own_window
    for axis in reversed(CTX[1:]):
        window_block = lax.all_gather(window_block, axis, axis=0, tiled=True)
    earlier = from_behind(window_block, CTX[0], 1)
    frame = jnp.concatenate([earlier, window_block], axis=0)
    gathered, inputs_full, frame = lax.optimization_barrier((gathered, inputs_full, frame))
    ordered = (
        gathered.reshape(shard_count, row_count, 2 * key_width)
        .transpose(1, 0, 2)
        .reshape(total_rows, 2 * key_width)
    )
    order_table = stripe_order.reshape(shard_count, row_count)
    key_place = order_table.T.reshape(total_rows)
    key_segment = segment_of(segments, key_place)
    query_place = lax.dynamic_slice_in_dim(stripe_order, first_row, row_count)
    query_segment = segment_of(segments, query_place)
    queries = split_heads(queries_cross)
    out_grads = split_heads(outputs_grad)
    block_rows = row_count // QUERY_BLOCKS
    query_grads = []
    key_total = jnp.zeros((total_rows, key_width), jnp.float32)
    value_total = jnp.zeros((total_rows, key_width), jnp.float32)
    for block in range(QUERY_BLOCKS):
        low = block * block_rows
        reach = (low + block_rows) * stripe
        block_place = query_place[low : low + block_rows]
        block_segment = query_segment[low : low + block_rows]
        allowed = (key_place[None, :reach] <= block_place[:, None]) & (
            key_segment[None, :reach] == block_segment[:, None]
        )
        query_grad, key_grad, value_grad = attend_block(
            queries[:, low : low + block_rows],
            out_grads[:, low : low + block_rows],
            ordered[:reach, :key_width],
            ordered[:reach, key_width:],
            allowed,
        )
        query_grads.append(query_grad)
        pad = ((0, total_rows - reach), (0, 0))
        key_total = key_total + jnp.pad(key_grad, pad)
        value_total = value_total + jnp.pad(value_grad, pad)
    grad_cross = join_heads(jnp.concatenate(query_grads, axis=1)).astype(jnp.bfloat16)

    partial = jnp.concatenate([key_total, value_total], axis=1).astype(jnp.bfloat16)
    sizes = tuple(lax.axis_size(axis) for axis in CTX)
    summed = partial.reshape(sizes + (row_count, 2 * key_width))
    for place in reversed(range(len(CTX))):
        arrived = lax.all_to_all(summed, CTX[place], split_axis=place, concat_axis=place, tiled=True)
        summed = jnp.sum(arrived.astype(jnp.float32), axis=place).astype(jnp.bfloat16)
    per_shard = row_count // stripe
    held_place = (
        lax.dynamic_slice_in_dim(order_table, shard_index * per_shard, per_shard, axis=1)
        .T.reshape(row_count)
    )
    local_place = held_place - first_row
    placement = (
        local_place[None, :] == jnp.arange(row_count, dtype=jnp.int32)[:, None]
    ).astype(jnp.bfloat16)
    shared_grad = jnp.dot(placement, summed, preferred_element_type=jnp.float32).astype(
        jnp.bfloat16
    )

    contract = (((1,), (1,)), ((), ()))
    normed_part = lax.dot_general(
        shared_grad[:, :key_width], weight_key, contract, preferred_element_type=jnp.float32
    )
    normed_part = normed_part + lax.dot_general(
        shared_grad[:, key_width:], weight_value, contract, preferred_element_type=jnp.float32
    )
    inputs_full = inputs_full.astype(jnp.float32)
    square_sum = jnp.sum(inputs_full * inputs_full, axis=1)
    inner_part = jnp.sum(normed_part * norm_gain[None, :] * inputs_full, axis=1)
    head_count = normed_part.shape[1] // column_count
    extra = jnp.tile(jnp.pad(inner_part, (0, column_count - row_count)), head_count)
    reduced = jnp.concatenate([normed_part, extra[None, :]], axis=0)
    in_block = shard_index % (window_block.shape[0] // row_count)
    window_all = lax.dynamic_slice_in_dim(frame, in_block * row_count, WINDOW + row_count)
    own_place = first_row + jnp.arange(row_count, dtype=jnp.int32)
    window_place = first_row - WINDOW + jnp.arange(WINDOW + row_count, dtype=jnp.int32)
    padded = jnp.concatenate([jnp.full((WINDOW,), -1, jnp.int32), segments])
    window_segment = lax.dynamic_slice_in_dim(padded, first_row, WINDOW + row_count)
    own_segment = lax.dynamic_slice_in_dim(segments, first_row, row_count)
    allowed = (
        (window_place[None, :] <= own_place[:, None])
        & (window_place[None, :] > own_place[:, None] - WINDOW)
        & (window_segment[None, :] == own_segment[:, None])
    )
    window_queries = split_heads(queries_window)
    window_weights, window_low, window_out = attend_forward(
        window_queries, window_all[:, :key_width], window_all[:, key_width:], allowed
    )
    reduced = lax.psum_scatter(reduced, HEAD[0], scatter_dimension=1, tiled=True)
    reduced, window_weights, window_low, window_out = lax.optimization_barrier(
        (reduced, window_weights, window_low, window_out)
    )
    for axis in HEAD[1:]:
        reduced = lax.psum_scatter(reduced, axis, scatter_dimension=1, tiled=True)
    normed_cols = reduced[:row_count]
    inner_sum = reduced[row_count, :row_count]
    gain_cols = lax.dynamic_slice_in_dim(
        norm_gain, lax.axis_index(HEAD) * column_count, column_count
    )
    inputs = norm_input.astype(jnp.float32)
    gained = normed_cols * gain_cols[None, :]
    scaling = lax.rsqrt(square_sum / D + 1e-06)[:, None]
    stream = (
        scaling * gained
        - inputs * scaling**3 * (inner_sum / D)[:, None]
        + upstream.astype(jnp.float32)
    )
    grad_stream = stream.astype(jnp.bfloat16)
    stream_full = grad_stream
    for axis in reversed(HEAD):
        stream_full = lax.all_gather(stream_full, axis, axis=1, tiled=True)
    head_grads = lax.dot_general(
        stream_full, weight_out, contract, preferred_element_type=jnp.float32
    ).astype(jnp.bfloat16)

    reach_count = WINDOW // row_count
    window_qgrad, window_kgrad, window_vgrad = attend_backward(
        window_queries,
        split_heads(head_grads),
        window_all[:, :key_width],
        window_all[:, key_width:],
        window_weights,
        window_low,
        window_out,
    )
    grad_queries = join_heads(window_qgrad).astype(jnp.bfloat16)
    window_part = jnp.concatenate([window_kgrad, window_vgrad], axis=1)
    collected = window_part[WINDOW:]
    for distance in range(1, reach_count + 1):
        lower_row = (reach_count - distance) * row_count
        collected = collected + from_behind(
            window_part[lower_row : lower_row + row_count], CTX, -distance
        )
    grad_keys = collected[:, :key_width].astype(jnp.bfloat16)
    grad_values = collected[:, key_width:].astype(jnp.bfloat16)
    return (grad_cross, grad_stream, grad_queries, grad_keys, grad_values)


def solution(mesh):
    ctx_parts = (mesh.shape["ctx"] // 8, 4, 2)
    head_parts = (2, mesh.shape["head"] // 2)
    parts = jax.sharding.Mesh(
        mesh.devices.reshape(ctx_parts + head_parts), CTX + HEAD
    )
    rows = P(CTX, HEAD)
    in_specs = (
        rows,
        rows,
        rows,
        rows,
        P(),
        P(),
        rows,
        P(),
        P(None, HEAD),
        P(None, HEAD),
        rows,
        P(HEAD, None),
        rows,
        rows,
        rows,
    )
    out_specs = (rows, rows, rows, rows, rows)
    return jax.shard_map(local, mesh=parts, in_specs=in_specs, out_specs=out_specs, check_vma=False)
```
